256 devices in a mesh: head: 8 (over z), vocab: 32 (over y, x, core).
Axes of the slice: x: 4, y: 4, z: 8, core: 2. Of those that a mesh axis runs over, the one named last changes fastest.
Arguments:
- hidden_states: bfloat16 [2048, 8192], P(('head', 'vocab')), may hold values from -6 to 6
- head_weight: bfloat16 [8, 8192, 16384], P('head', None, 'vocab'), may hold values from -1 to 1
- tags: int32 [2048, 1], P(('head', 'vocab')), may hold values from 0 to 7; in each aligned block of 8 rows (0 to 7, 8 to 15, ...) at most 2 rows name the same one
- targets: int32 [2048], P(('head', 'vocab')), may hold values from 0 to 16383
- row_grad: bfloat16 [2048], P(('head', 'vocab')), may hold values from -192 to 192
Outputs:
- row_loss: bfloat16 [2048], P(('head', 'vocab'))
- hidden_grad: bfloat16 [2048, 8192], P(('head', 'vocab'))
The draws below stay inside these ranges and needn't reach their ends.
Inputs may be any that keep to these rules, and one draw needn't show every extreme that they name: `tags`: in each aligned block of 8 rows (the rows of one device) no head is named by more than 2 rows, and in every draw some block has exactly 2 rows of one head.
All inputs are finite; a program needn't handle non-finite values.
Results may differ from the reference program's by a relative error of at most 0.018.
Values may be sent and summed in bfloat16 or wider, within the bound.
No kernel may reach another device: no remote copies, remote signals or barrier semaphores. Data moves between devices by JAX's collectives and lax.ppermute only.
A program may use at most 64 MiB of HBM per device.

```python
import math
import jax
import jax.numpy as jnp
import numpy as np
from jax import lax

D = 8192
VOCAB = 16384
ROW_DEV = 8
CAP = 2
HEADS = 8
ROWS = 2048
N_VOCAB = 32


def base_hidden(key):
    return jnp.clip(jax.random.normal(jax.random.fold_in(key, 71), (ROWS, D), jnp.float32), -6.0, 6.0)


def draw_hidden_states(key, part):
    values = base_hidden(key)
    return values.astype(jnp.bfloat16)


def draw_head_weight(key, part):
    values = jnp.clip(jax.random.normal(jax.random.fold_in(key, 73), (HEADS, D, VOCAB), jnp.float32), -6.0, 6.0) * D ** (-0.5)
    return values.astype(jnp.bfloat16)


def place_ends(result, stream_key, smallest, top_value):
    place = [jax.random.randint(jax.random.fold_in(stream_key, axis), (), 0, length) for axis, length in enumerate(result.shape)]
    main_axis = result.shape.index(max(result.shape))
    neighbour = place[:main_axis] + [(place[main_axis] + 1) % result.shape[main_axis]] + place[main_axis + 1:]
    return result.at[tuple(place)].set(smallest).at[tuple(neighbour)].set(top_value)


def block_scale(key, shape, split, low, high):
    def one(axis_at, blocks):
        heights = jax.random.uniform(jax.random.fold_in(jax.random.fold_in(key, 6), axis_at), (blocks,), jnp.float32, low / len(split), high / len(split))
        return jnp.repeat(jnp.exp(heights), shape[axis_at] // blocks).reshape((-1,) + (1,) * (len(shape) - axis_at - 1))

    level = one(*split[0])
    for cut in split[1:]:
        level = level * one(*cut)
    return level


def shared_out(key, own, number, rows, count, top, most, lean):
    sequence = jax.random.permutation(key, count)
    crowded, usual = load_shares(count, rows * top, most, lean, True), load_shares(count, rows * top, most, lean, False)
    places = jnp.arange(count)

    def named(tallies, offset_by):
        used = int((tallies > 0).sum())
        fixed = max(1, used // 4)
        moved = fixed + (places - fixed + offset_by * (used - fixed)) % max(1, count - fixed)
        return jnp.zeros((count,), jnp.int32).at[sequence[jnp.where(places < fixed, places, moved)]].set(jnp.asarray(tallies, jnp.int32))

    tallies = jnp.where(number % 4 == 0, named(crowded, number // 4), named(usual, number - number // 4 - 1))
    mixed = jax.random.permutation(jax.random.fold_in(own, 3), count)
    donor, sink = mixed[0:count // 2 * 2:2], mixed[1:count // 2 * 2:2]
    room = jnp.minimum(tallies[donor] - 1, most - tallies[sink]) // 2
    room = jnp.where((donor == sequence[0]) | (sink == sequence[0]) | (tallies[sink] == 0), 0, jnp.maximum(room, 0))
    moved = jax.random.randint(jax.random.fold_in(own, 4), (count // 2,), 0, 1 << 20) % (room + 1)
    tallies = tallies.at[donor].add(-moved).at[sink].add(moved)
    members = jnp.searchsorted(jnp.cumsum(tallies), jnp.arange(rows * top), side="right").astype(jnp.int32)
    grid = members.reshape(top, rows).T
    grid = grid[jax.random.permutation(jax.random.fold_in(own, 1), rows)]
    offset_by = jax.random.randint(jax.random.fold_in(own, 2), (rows, 1), 0, top)
    return jnp.take_along_axis(grid, (jnp.arange(top)[None, :] + offset_by) % top, axis=1)


def load_shares(amount, total, limit, slope, full):
    portions = [(1 << 20) // math.isqrt(grade ** slope) + 1 for grade in range(1, amount + 1)]
    largest = limit if full else min(limit, max(-(-total // amount), total * portions[0] // sum(portions)))
    least = 1 if total - largest >= amount - 1 else 0
    given, surplus = [largest] + [least] * (amount - 1), total - largest - least * (amount - 1)
    while surplus > 0:
        free = [i for i in range(1, amount) if given[i] < largest] or [i for i in range(1, amount) if given[i] < limit]
        whole, remaining = sum([portions[i] for i in free]), surplus
        for i in free:
            extra = min(limit - given[i], max(1, remaining * portions[i] // whole), surplus)
            given[i] = given[i] + extra
            surplus = surplus - extra
    return np.array(given)


def normal_values(key, extent, scale, reach, shards=(), held_as=jnp.bfloat16):
    entries = scale * jax.random.normal(key, extent, jnp.float32)
    if shards:
        entries = entries * block_scale(key, extent, shards, -0.22, 0.18)
    return jnp.clip(entries, -reach, reach).astype(held_as)


def setup_inputs(seed: int = 0) -> dict:
    seeds = jax.random.split(jax.random.key(seed), 6)
    hidden_states = draw_hidden_states(jax.random.fold_in(seeds[5], 71), 0)
    head_weight = draw_head_weight(jax.random.fold_in(seeds[5], 71), 0)
    tags_keys = jax.random.split(jax.random.fold_in(seeds[2], 1), ROWS // ROW_DEV)
    tags_turns = jax.random.permutation(jax.random.fold_in(seeds[2], 3), ROWS // ROW_DEV)
    tags = jax.vmap(lambda own, number: shared_out(jax.random.fold_in(seeds[2], 2), own, number, ROW_DEV, HEADS, 1, CAP, 2))(tags_keys, tags_turns).reshape((ROWS, 1))
    targets = place_ends(jax.random.randint(seeds[3], (ROWS,), 0, VOCAB), jax.random.fold_in(seeds[3], 1), 0, VOCAB - 1).astype(jnp.int32)
    row_grad = normal_values(seeds[4], (ROWS,), 32.0, 192.0, ((0, 256),))
    return dict(hidden_states=hidden_states, head_weight=head_weight, tags=tags, targets=targets, row_grad=row_grad)


block_rows = 64


def reference(hidden_states, head_weight, tags, targets, row_grad):
    row_tag = tags[:, 0].astype(jnp.int32)
    row_order = jnp.argsort(row_tag, stable=True).astype(jnp.int32)
    head_ids = jnp.arange(HEADS, dtype=jnp.int32)
    counts = jnp.sum((row_tag[:, None] == head_ids[None, :]).astype(jnp.int32), axis=0).astype(jnp.int32)
    starts = (jnp.cumsum(counts) - counts).astype(jnp.int32)
    sorted_rows = jnp.concatenate([hidden_states[row_order], jnp.zeros((block_rows, D), hidden_states.dtype)], 0)
    sorted_targets = jnp.concatenate([targets[row_order].astype(jnp.int32), jnp.zeros((block_rows,), jnp.int32)], 0)
    sorted_scale = jnp.concatenate([row_grad[row_order].astype(jnp.float32), jnp.zeros((block_rows,), jnp.float32)], 0)
    loss_sorted = jnp.zeros((ROWS + block_rows,), jnp.float32)
    grad_sorted = jnp.zeros((ROWS + block_rows, D), jnp.bfloat16)
    position = jnp.arange(block_rows, dtype=jnp.int32)
    columns = jnp.arange(VOCAB, dtype=jnp.int32)
    for head in range(HEADS):
        weight = head_weight[head]
        weight_wide = weight.astype(jnp.float32).reshape(D, N_VOCAB, VOCAB // N_VOCAB)
        first_row = starts[head]
        last_row = (starts[head] + counts[head]).astype(jnp.int32)
        block_count = ((counts[head] + block_rows - 1) // block_rows).astype(jnp.int32)

        def block_step(index, carry, weight=weight, weight_wide=weight_wide, first_row=first_row, last_row=last_row):
            loss_now, grad_now = carry
            begin = (first_row + index * block_rows).astype(jnp.int32)
            rows_block = lax.dynamic_slice(sorted_rows, (begin, jnp.int32(0)), (block_rows, D))
            target_block = lax.dynamic_slice(sorted_targets, (begin,), (block_rows,))
            scale_block = lax.dynamic_slice(sorted_scale, (begin,), (block_rows,))
            logits = jnp.dot(rows_block, weight, preferred_element_type=jnp.float32)
            row_top = jnp.max(logits, axis=1)
            shifted = jnp.exp(logits - row_top[:, None])
            row_total = jnp.sum(shifted, axis=1)
            target_hit = columns[None, :] == target_block[:, None]
            target_logit = jnp.sum(jnp.where(target_hit, logits, 0.0), axis=1)
            loss_block = (jnp.log(row_total) + row_top - target_logit).astype(jnp.bfloat16)
            probabilities = shifted / row_total[:, None]
            dlogits = (scale_block[:, None] * (probabilities - target_hit.astype(jnp.float32))).astype(jnp.bfloat16)
            partials = jnp.einsum('rvk,dvk->vrd', dlogits.astype(jnp.float32).reshape(block_rows, N_VOCAB, VOCAB // N_VOCAB), weight_wide)
            rounded = lax.optimization_barrier(partials.astype(jnp.bfloat16))
            grad_block = jnp.sum(rounded.astype(jnp.float32), axis=0).astype(jnp.bfloat16)
            live_rows = (begin + position) < last_row
            old_loss = lax.dynamic_slice(loss_now, (begin,), (block_rows,))
            new_loss = jnp.where(live_rows, loss_block.astype(jnp.float32), old_loss)
            loss_now = lax.dynamic_update_slice(loss_now, new_loss, (begin,))
            old_grad = lax.dynamic_slice(grad_now, (begin, jnp.int32(0)), (block_rows, D))
            new_grad = jnp.where(live_rows[:, None], grad_block, old_grad)
            grad_now = lax.dynamic_update_slice(grad_now, new_grad, (begin, jnp.int32(0)))
            return (loss_now, grad_now)

        loss_sorted, grad_sorted = lax.fori_loop(jnp.int32(0), block_count, block_step, (loss_sorted, grad_sorted))
    row_loss = jnp.zeros((ROWS,), jnp.float32).at[row_order].set(loss_sorted[:ROWS]).astype(jnp.bfloat16)
    hidden_grad = jnp.zeros((ROWS, D), jnp.bfloat16).at[row_order].set(grad_sorted[:ROWS])
    return (row_loss, hidden_grad)
```

```python
import jax
import jax.numpy as jnp
from jax import lax
from jax.sharding import PartitionSpec as P

CAP = 2
META = 128


def per_device(hidden_states, head_weight, tags, targets, row_grad):
    head_count = lax.axis_size("head")
    own_rows = head_count * CAP
    width = hidden_states.shape[1]
    row_tag = tags[:, 0]
    local_rows = row_tag.shape[0]
    row_iota = lax.broadcasted_iota(jnp.int32, (local_rows, local_rows), 0)
    col_iota = lax.broadcasted_iota(jnp.int32, (local_rows, local_rows), 1)
    earlier = (row_tag[None, :] == row_tag[:, None]) & (col_iota < row_iota)
    slot_rank = jnp.sum(earlier.astype(jnp.int32), axis=1)
    slot_index = row_tag * CAP + slot_rank
    selector = jnp.arange(own_rows, dtype=jnp.int32)[:, None] == slot_index[None, :]

    meta_col = lax.broadcasted_iota(jnp.int32, (local_rows, META), 1)
    t = targets[:, None]
    meta = jnp.where(
        meta_col == 0,
        (t >> 7).astype(jnp.float32),
        jnp.where(
            meta_col == 1,
            (t & 127).astype(jnp.float32),
            jnp.where(meta_col == 2, row_grad[:, None].astype(jnp.float32), 0.0),
        ),
    ).astype(jnp.bfloat16)
    payload = jnp.concatenate([hidden_states, meta], axis=1)
    send = jnp.dot(
        selector.astype(jnp.bfloat16), payload, preferred_element_type=jnp.float32
    ).astype(jnp.bfloat16)

    arrived = lax.all_to_all(send, "head", split_axis=0, concat_axis=0, tiled=True)
    gathered = lax.all_gather(arrived, "vocab", axis=0, tiled=True)
    group_targets = (
        gathered[:, width].astype(jnp.int32) * 128 + gathered[:, width + 1].astype(jnp.int32)
    )
    group_scale = gathered[:, width + 2].astype(jnp.float32)

    weight = head_weight[0]
    vocab_width = weight.shape[1]
    logits = jnp.dot(gathered[:, :width], weight, preferred_element_type=jnp.float32)
    offset = lax.axis_index("vocab") * vocab_width
    target_hit = lax.broadcasted_iota(jnp.int32, logits.shape, 1) + offset == group_targets[:, None]
    own_target = jnp.sum(jnp.where(target_hit, logits, 0.0), axis=1)
    local_top = jnp.max(logits, axis=1)
    local_total = jnp.sum(jnp.exp(logits - local_top[:, None]), axis=1)
    stats = jnp.stack([local_top, local_total, own_target], axis=0)
    all_stats = lax.all_gather(stats, "vocab", axis=0, tiled=False)
    row_top = jnp.max(all_stats[:, 0, :], axis=0)
    row_total = jnp.sum(all_stats[:, 1, :] * jnp.exp(all_stats[:, 0, :] - row_top[None, :]), axis=0)
    target_logit = jnp.sum(all_stats[:, 2, :], axis=0)
    group_loss = jnp.log(row_total) + row_top - target_logit
    probabilities = jnp.exp(logits - row_top[:, None]) / row_total[:, None]
    dlogits = (group_scale[:, None] * (probabilities - target_hit.astype(jnp.float32))).astype(
        jnp.bfloat16
    )
    partial_value = lax.dot_general(
        dlogits, weight, (((1,), (1,)), ((), ())), preferred_element_type=jnp.float32
    ).astype(jnp.bfloat16)
    own_grad = lax.psum_scatter(partial_value, "vocab", scatter_dimension=0, tiled=True)
    own_loss = lax.dynamic_slice_in_dim(group_loss, lax.axis_index("vocab") * own_rows, own_rows, 0)
    back_meta = jnp.where(
        lax.broadcasted_iota(jnp.int32, (own_rows, META), 1) == 0, own_loss[:, None], 0.0
    ).astype(jnp.bfloat16)
    back = jnp.concatenate([own_grad, back_meta], axis=1)
    returned = lax.all_to_all(back, "head", split_axis=0, concat_axis=0, tiled=True)
    restored = jnp.dot(
        selector.T.astype(jnp.bfloat16), returned, preferred_element_type=jnp.float32
    ).astype(jnp.bfloat16)
    hidden_grad = restored[:, :width]
    row_loss = restored[:, width]
    return (row_loss, hidden_grad)


def solution(mesh):
    placed = (
        P(("head", "vocab"), None),
        P("head", None, "vocab"),
        P(("head", "vocab"), None),
        P(("head", "vocab")),
        P(("head", "vocab")),
    )
    return jax.shard_map(
        per_device,
        mesh=mesh,
        in_specs=placed,
        out_specs=(P(("head", "vocab")), P(("head", "vocab"), None)),
        check_vma=False,
    )
```

```python
import jax
import jax.numpy as jnp
from jax import lax
from jax.sharding import PartitionSpec as P

CAP = 2
META = 128


def per_device(hidden_states, head_weight, tags, targets, row_grad):
    head_count = lax.axis_size("head")
    own_rows = head_count * CAP
    width = hidden_states.shape[1]
    row_tag = tags[:, 0]
    local_rows = row_tag.shape[0]
    row_iota = lax.broadcasted_iota(jnp.int32, (local_rows, local_rows), 0)
    col_iota = lax.broadcasted_iota(jnp.int32, (local_rows, local_rows), 1)
    earlier = (row_tag[None, :] == row_tag[:, None]) & (col_iota < row_iota)
    slot_rank = jnp.sum(earlier.astype(jnp.int32), axis=1)
    slot_index = row_tag * CAP + slot_rank
    selector = jnp.arange(own_rows, dtype=jnp.int32)[:, None] == slot_index[None, :]

    meta_col = lax.broadcasted_iota(jnp.int32, (local_rows, META), 1)
    t = targets[:, None]
    meta = jnp.where(
        meta_col == 0,
        (t >> 7).astype(jnp.float32),
        jnp.where(
            meta_col == 1,
            (t & 127).astype(jnp.float32),
            jnp.where(meta_col == 2, row_grad[:, None].astype(jnp.float32), 0.0),
        ),
    ).astype(jnp.bfloat16)
    payload = jnp.concatenate([hidden_states, meta], axis=1)
    send = jnp.dot(
        selector.astype(jnp.bfloat16), payload, preferred_element_type=jnp.float32
    ).astype(jnp.bfloat16)

    arrived = lax.all_to_all(send, "head", split_axis=0, concat_axis=0, tiled=True)
    gathered = lax.all_gather(arrived, "chip", axis=0, tiled=True)
    gathered = lax.all_gather(gathered, "core", axis=0, tiled=True)
    group_targets = (
        gathered[:, width].astype(jnp.int32) * 128 + gathered[:, width + 1].astype(jnp.int32)
    )
    group_scale = gathered[:, width + 2].astype(jnp.float32)

    weight = head_weight[0]
    vocab_width = weight.shape[1]
    logits = jnp.dot(gathered[:, :width], weight, preferred_element_type=jnp.float32)
    vocab_index = lax.axis_index("chip") * lax.axis_size("core") + lax.axis_index("core")
    offset = vocab_index * vocab_width
    target_hit = lax.broadcasted_iota(jnp.int32, logits.shape, 1) + offset == group_targets[:, None]
    own_target = jnp.sum(jnp.where(target_hit, logits, 0.0), axis=1)
    local_top = jnp.max(logits, axis=1)
    local_total = jnp.sum(jnp.exp(logits - local_top[:, None]), axis=1)
    stats = jnp.stack([local_top, local_total, own_target], axis=0)
    all_stats = lax.all_gather(stats, ("chip", "core"), axis=0, tiled=False)
    row_top = jnp.max(all_stats[:, 0, :], axis=0)
    row_total = jnp.sum(all_stats[:, 1, :] * jnp.exp(all_stats[:, 0, :] - row_top[None, :]), axis=0)
    target_logit = jnp.sum(all_stats[:, 2, :], axis=0)
    group_loss = jnp.log(row_total) + row_top - target_logit
    probabilities = jnp.exp(logits - row_top[:, None]) / row_total[:, None]
    dlogits = (group_scale[:, None] * (probabilities - target_hit.astype(jnp.float32))).astype(
        jnp.bfloat16
    )
    partial_value = lax.dot_general(
        dlogits, weight, (((1,), (1,)), ((), ())), preferred_element_type=jnp.float32
    ).astype(jnp.bfloat16)
    half = lax.psum_scatter(partial_value, "core", scatter_dimension=0, tiled=True)
    own_grad = lax.psum_scatter(half, "chip", scatter_dimension=0, tiled=True)
    own_start = (lax.axis_index("core") * lax.axis_size("chip") + lax.axis_index("chip")) * own_rows
    own_loss = lax.dynamic_slice_in_dim(group_loss, own_start, own_rows, 0)
    back_meta = jnp.where(
        lax.broadcasted_iota(jnp.int32, (own_rows, META), 1) == 0, own_loss[:, None], 0.0
    ).astype(jnp.bfloat16)
    back = jnp.concatenate([own_grad, back_meta], axis=1)
    returned = lax.all_to_all(back, "head", split_axis=0, concat_axis=0, tiled=True)
    restored = jnp.dot(
        selector.T.astype(jnp.bfloat16), returned, preferred_element_type=jnp.float32
    ).astype(jnp.bfloat16)
    hidden_grad = restored[:, :width]
    row_loss = restored[:, width]
    return (row_loss, hidden_grad)


def solution(mesh):
    heads, vocab = mesh.devices.shape
    split = jax.sharding.Mesh(mesh.devices.reshape(heads, vocab // 2, 2), ("head", "chip", "core"))
    rows = ("head", "chip", "core")
    placed = (
        P(rows, None),
        P("head", None, ("chip", "core")),
        P(rows, None),
        P(rows),
        P(rows),
    )
    return jax.shard_map(
        per_device,
        mesh=split,
        in_specs=placed,
        out_specs=(P(rows), P(rows, None)),
        check_vma=False,
    )
```

```python
import jax
import jax.numpy as jnp
from jax import lax
from jax.sharding import PartitionSpec as P

CAP = 2
META = 128


def per_device(hidden_states, head_weight, tags, targets, row_grad):
    head_count = lax.axis_size("head")
    own_rows = head_count * CAP
    width = hidden_states.shape[1]
    row_tag = tags[:, 0]
    local_rows = row_tag.shape[0]
    row_iota = lax.broadcasted_iota(jnp.int32, (local_rows, local_rows), 0)
    col_iota = lax.broadcasted_iota(jnp.int32, (local_rows, local_rows), 1)
    earlier = (row_tag[None, :] == row_tag[:, None]) & (col_iota < row_iota)
    slot_rank = jnp.sum(earlier.astype(jnp.int32), axis=1)
    slot_index = row_tag * CAP + slot_rank
    selector = jnp.arange(own_rows, dtype=jnp.int32)[:, None] == slot_index[None, :]

    meta_col = lax.broadcasted_iota(jnp.int32, (local_rows, META), 1)
    t = targets[:, None]
    meta = jnp.where(
        meta_col == 0,
        (t >> 7).astype(jnp.float32),
        jnp.where(
            meta_col == 1,
            (t & 127).astype(jnp.float32),
            jnp.where(meta_col == 2, row_grad[:, None].astype(jnp.float32), 0.0),
        ),
    ).astype(jnp.bfloat16)
    payload = jnp.concatenate([hidden_states, meta], axis=1)
    send = jnp.dot(
        selector.astype(jnp.bfloat16), payload, preferred_element_type=jnp.float32
    ).astype(jnp.bfloat16)

    arrived = lax.all_to_all(send, "head", split_axis=0, concat_axis=0, tiled=True)
    gathered = lax.all_gather(arrived, "vocab", axis=0, tiled=True)
    group_targets = (
        gathered[:, width].astype(jnp.int32) * 128 + gathered[:, width + 1].astype(jnp.int32)
    )
    group_scale = gathered[:, width + 2].astype(jnp.float32)

    weight = head_weight[0]
    vocab_width = weight.shape[1]
    logits = jnp.dot(gathered[:, :width], weight, preferred_element_type=jnp.float32)
    offset = lax.axis_index("vocab") * vocab_width
    target_hit = lax.broadcasted_iota(jnp.int32, logits.shape, 1) + offset == group_targets[:, None]
    own_target = jnp.sum(jnp.where(target_hit, logits, 0.0), axis=1)
    local_top = jnp.max(logits, axis=1)
    local_total = jnp.sum(jnp.exp(logits - local_top[:, None]), axis=1)
    stats = jnp.stack([local_top, local_total, own_target], axis=0)
    copies = jnp.broadcast_to(stats[None], (lax.axis_size("vocab"),) + stats.shape)
    all_stats = lax.all_to_all(copies, "vocab", split_axis=0, concat_axis=0, tiled=True)
    row_top = jnp.max(all_stats[:, 0, :], axis=0)
    row_total = jnp.sum(all_stats[:, 1, :] * jnp.exp(all_stats[:, 0, :] - row_top[None, :]), axis=0)
    target_logit = jnp.sum(all_stats[:, 2, :], axis=0)
    group_loss = jnp.log(row_total) + row_top - target_logit
    probabilities = jnp.exp(logits - row_top[:, None]) / row_total[:, None]
    dlogits = (group_scale[:, None] * (probabilities - target_hit.astype(jnp.float32))).astype(
        jnp.bfloat16
    )
    partial_value = lax.dot_general(
        dlogits, weight, (((1,), (1,)), ((), ())), preferred_element_type=jnp.float32
    ).astype(jnp.bfloat16)
    own_grad = lax.psum_scatter(partial_value, "vocab", scatter_dimension=0, tiled=True)
    own_loss = lax.dynamic_slice_in_dim(group_loss, lax.axis_index("vocab") * own_rows, own_rows, 0)
    back_meta = jnp.where(
        lax.broadcasted_iota(jnp.int32, (own_rows, META), 1) == 0, own_loss[:, None], 0.0
    ).astype(jnp.bfloat16)
    back = jnp.concatenate([own_grad, back_meta], axis=1)
    returned = lax.all_to_all(back, "head", split_axis=0, concat_axis=0, tiled=True)
    restored = jnp.dot(
        selector.T.astype(jnp.bfloat16), returned, preferred_element_type=jnp.float32
    ).astype(jnp.bfloat16)
    hidden_grad = restored[:, :width]
    row_loss = restored[:, width]
    return (row_loss, hidden_grad)


def solution(mesh):
    placed = (
        P(("head", "vocab"), None),
        P("head", None, "vocab"),
        P(("head", "vocab"), None),
        P(("head", "vocab")),
        P(("head", "vocab")),
    )
    return jax.shard_map(
        per_device,
        mesh=mesh,
        in_specs=placed,
        out_specs=(P(("head", "vocab")), P(("head", "vocab"), None)),
        check_vma=False,
    )
```

```python
import jax
import jax.numpy as jnp
from jax import lax
from jax.sharding import PartitionSpec as P

CAP = 2
META = 128


def per_device(hidden_states, head_weight, tags, targets, row_grad):
    head_count = lax.axis_size("head")
    own_rows = head_count * CAP
    width = hidden_states.shape[1]
    row_tag = tags[:, 0]
    local_rows = row_tag.shape[0]
    row_iota = lax.broadcasted_iota(jnp.int32, (local_rows, local_rows), 0)
    col_iota = lax.broadcasted_iota(jnp.int32, (local_rows, local_rows), 1)
    earlier = (row_tag[None, :] == row_tag[:, None]) & (col_iota < row_iota)
    slot_rank = jnp.sum(earlier.astype(jnp.int32), axis=1)
    slot_index = row_tag * CAP + slot_rank
    selector = jnp.arange(own_rows, dtype=jnp.int32)[:, None] == slot_index[None, :]

    meta_col = lax.broadcasted_iota(jnp.int32, (local_rows, META), 1)
    t = targets[:, None]
    meta = jnp.where(
        meta_col == 0,
        (t >> 7).astype(jnp.float32),
        jnp.where(
            meta_col == 1,
            (t & 127).astype(jnp.float32),
            jnp.where(meta_col == 2, row_grad[:, None].astype(jnp.float32), 0.0),
        ),
    ).astype(jnp.bfloat16)
    payload = jnp.concatenate([hidden_states, meta], axis=1)
    send = jnp.dot(
        selector.astype(jnp.bfloat16), payload, preferred_element_type=jnp.float32
    ).astype(jnp.bfloat16)

    arrived = lax.all_to_all(send, "head", split_axis=0, concat_axis=0, tiled=True)
    gathered = lax.all_gather(arrived, "vocab", axis=0, tiled=True)
    group_targets = (
        gathered[:, width].astype(jnp.int32) * 128 + gathered[:, width + 1].astype(jnp.int32)
    )
    group_scale = gathered[:, width + 2].astype(jnp.float32)

    weight = head_weight[0]
    vocab_width = weight.shape[1]
    logits = jnp.dot(gathered[:, :width], weight, preferred_element_type=jnp.float32)
    offset = lax.axis_index("vocab") * vocab_width
    target_hit = lax.broadcasted_iota(jnp.int32, logits.shape, 1) + offset == group_targets[:, None]
    own_target = jnp.sum(jnp.where(target_hit, logits, 0.0), axis=1)
    local_top = jnp.max(logits, axis=1)
    local_total = jnp.sum(jnp.exp(logits - local_top[:, None]), axis=1)
    stats = jnp.stack([local_top, local_total, own_target], axis=0)
    copies = jnp.broadcast_to(stats[None], (lax.axis_size("vocab"),) + stats.shape)
    all_stats = lax.all_to_all(copies, "vocab", split_axis=0, concat_axis=0, tiled=True)
    row_top = jnp.max(all_stats[:, 0, :], axis=0)
    row_total = jnp.sum(all_stats[:, 1, :] * jnp.exp(all_stats[:, 0, :] - row_top[None, :]), axis=0)
    target_logit = jnp.sum(all_stats[:, 2, :], axis=0)
    group_loss = jnp.log(row_total) + row_top - target_logit
    probabilities = jnp.exp(logits - row_top[:, None]) / row_total[:, None]
    dlogits = (group_scale[:, None] * (probabilities - target_hit.astype(jnp.float32))).astype(
        jnp.bfloat16
    )
    partial_value = lax.dot_general(
        dlogits, weight, (((1,), (1,)), ((), ())), preferred_element_type=jnp.float32
    ).astype(jnp.bfloat16)
    own_grad = lax.psum_scatter(partial_value, "vocab", scatter_dimension=0, tiled=True)
    own_loss = lax.dynamic_slice_in_dim(group_loss, lax.axis_index("vocab") * own_rows, own_rows, 0)
    back_meta = jnp.where(
        lax.broadcasted_iota(jnp.int32, (own_rows, META), 1) == 0, own_loss[:, None], 0.0
    ).astype(jnp.bfloat16)
    returned_meta = lax.all_to_all(back_meta, "head", split_axis=0, concat_axis=0, tiled=True)
    row_loss = jnp.dot(
        selector.T.astype(jnp.bfloat16), returned_meta, preferred_element_type=jnp.float32
    ).astype(jnp.bfloat16)[:, 0]
    returned = lax.all_to_all(own_grad, "head", split_axis=0, concat_axis=0, tiled=True)
    hidden_grad = jnp.dot(
        selector.T.astype(jnp.bfloat16), returned, preferred_element_type=jnp.float32
    ).astype(jnp.bfloat16)
    return (row_loss, hidden_grad)


def solution(mesh):
    placed = (
        P(("head", "vocab"), None),
        P("head", None, "vocab"),
        P(("head", "vocab"), None),
        P(("head", "vocab")),
        P(("head", "vocab")),
    )
    return jax.shard_map(
        per_device,
        mesh=mesh,
        in_specs=placed,
        out_specs=(P(("head", "vocab")), P(("head", "vocab"), None)),
        check_vma=False,
    )
```

```python
import jax
import jax.numpy as jnp
from jax import lax
from jax.sharding import PartitionSpec as P

CAP = 2
META = 128


def per_device(hidden_states, head_weight, tags, targets, row_grad):
    head_count = lax.axis_size("head")
    own_rows = head_count * CAP
    width = hidden_states.shape[1]
    row_tag = tags[:, 0]
    local_rows = row_tag.shape[0]
    row_iota = lax.broadcasted_iota(jnp.int32, (local_rows, local_rows), 0)
    col_iota = lax.broadcasted_iota(jnp.int32, (local_rows, local_rows), 1)
    earlier = (row_tag[None, :] == row_tag[:, None]) & (col_iota < row_iota)
    slot_rank = jnp.sum(earlier.astype(jnp.int32), axis=1)
    slot_index = row_tag * CAP + slot_rank
    selector = jnp.arange(own_rows, dtype=jnp.int32)[:, None] == slot_index[None, :]

    fields = jnp.stack(
        [(targets >> 7).astype(jnp.bfloat16), (targets & 127).astype(jnp.bfloat16), row_grad], axis=1
    )
    meta = jnp.pad(fields, ((0, 0), (0, META - 3)))
    payload = jnp.concatenate([hidden_states, meta], axis=1)
    send = jnp.dot(
        selector.astype(jnp.bfloat16), payload, preferred_element_type=jnp.float32
    ).astype(jnp.bfloat16)

    arrived = lax.all_to_all(send, "head", split_axis=0, concat_axis=0, tiled=True)
    gathered = lax.all_gather(arrived, "vocab", axis=0, tiled=True)
    group_targets = (
        gathered[:, width].astype(jnp.int32) * 128 + gathered[:, width + 1].astype(jnp.int32)
    )
    group_scale = gathered[:, width + 2].astype(jnp.float32)

    weight = head_weight[0]
    vocab_width = weight.shape[1]
    logits = jnp.dot(gathered[:, :width], weight, preferred_element_type=jnp.float32)
    offset = lax.axis_index("vocab") * vocab_width
    target_hit = lax.broadcasted_iota(jnp.int32, logits.shape, 1) + offset == group_targets[:, None]
    own_target = jnp.sum(jnp.where(target_hit, logits, 0.0), axis=1)
    local_top = jnp.max(logits, axis=1)
    local_total = jnp.sum(jnp.exp(logits - local_top[:, None]), axis=1)
    stats = jnp.stack([local_top, local_total, own_target], axis=0)
    copies = jnp.broadcast_to(stats[None], (lax.axis_size("vocab"),) + stats.shape)
    all_stats = lax.all_to_all(copies, "vocab", split_axis=0, concat_axis=0, tiled=True)
    row_top = jnp.max(all_stats[:, 0, :], axis=0)
    row_total = jnp.sum(all_stats[:, 1, :] * jnp.exp(all_stats[:, 0, :] - row_top[None, :]), axis=0)
    target_logit = jnp.sum(all_stats[:, 2, :], axis=0)
    group_loss = jnp.log(row_total) + row_top - target_logit
    probabilities = jnp.exp(logits - row_top[:, None]) / row_total[:, None]
    dlogits = (group_scale[:, None] * (probabilities - target_hit.astype(jnp.float32))).astype(
        jnp.bfloat16
    )
    partial_value = lax.dot_general(
        dlogits, weight, (((1,), (1,)), ((), ())), preferred_element_type=jnp.float32
    ).astype(jnp.bfloat16)
    own_grad = lax.psum_scatter(partial_value, "vocab", scatter_dimension=0, tiled=True)
    own_loss = lax.dynamic_slice_in_dim(group_loss, lax.axis_index("vocab") * own_rows, own_rows, 0)
    back_meta = jnp.where(
        lax.broadcasted_iota(jnp.int32, (own_rows, META), 1) == 0, own_loss[:, None], 0.0
    ).astype(jnp.bfloat16)
    back = jnp.concatenate([own_grad, back_meta], axis=1)
    returned = lax.all_to_all(back, "head", split_axis=0, concat_axis=0, tiled=True)
    pick = selector.T.astype(jnp.bfloat16)
    hidden_grad = jnp.dot(pick, returned[:, :width], preferred_element_type=jnp.float32).astype(
        jnp.bfloat16
    )
    row_loss = jnp.dot(pick, returned[:, width:], preferred_element_type=jnp.float32)[:, 0].astype(
        jnp.bfloat16
    )
    return (row_loss, hidden_grad)


def solution(mesh):
    placed = (
        P(("head", "vocab"), None),
        P("head", None, "vocab"),
        P(("head", "vocab"), None),
        P(("head", "vocab")),
        P(("head", "vocab")),
    )
    return jax.shard_map(
        per_device,
        mesh=mesh,
        in_specs=placed,
        out_specs=(P(("head", "vocab")), P(("head", "vocab"), None)),
        check_vma=False,
    )
```
